256 devices in a mesh: space: 32 (over x, z), sub: 8 (over y, core).
Axes of the slice: x: 4, y: 4, z: 8, core: 2. Of those that a mesh axis runs over, the one named last changes fastest.
Arguments:
- offsets: float32 [32, 8, 32, 8, 4, 3, 128], P('space', 'sub'), may hold values from 0.5 to 7.5
- normals: float32 [32, 8, 32, 8, 4, 3, 128], P('space', 'sub'), may hold values from -6 to 6
- density: float32 [32, 8, 32, 8, 4, 128], P('space', 'sub'), may hold values from 0.3 to 3
- tile_brick: int32 [32, 8, 32, 8, 4], P('space', 'sub'), may hold values from 0 to 63
- tile_count: int32 [32, 8, 32, 8, 4], P('space', 'sub'), may hold values from 32 to 128, as said below
Outputs:
- indicator: float32 [512, 128, 128], P('space', 'sub')
- density_field: float32 [512, 128, 128], P('space', 'sub')
The draws below stay inside these ranges and needn't reach their ends.
Inputs may be any that keep to these rules, and one draw needn't show every extreme that they name: `tile_count`: slots at and beyond a tile's count are padding; some tile holds 128 live points.
All inputs are finite; a program needn't handle non-finite values.
Results may differ from the reference program's by a relative error of at most 0.0003.
Values sent between devices are 32-bit elements; how exact they have to be, the bound alone decides.
No kernel may reach another device: no remote copies, remote signals or barrier semaphores. Data moves between devices by JAX's collectives and lax.ppermute only.
A program may use at most 192 MiB of HBM per device.

```python
import math
import jax
import jax.numpy as jnp
from jax import lax

BRICK = 8
SLOTS = 128
TPD = 4
CX = 16
CY = 16
CZ = 128
LEVELS = 4
SWEEPS = 2
COARSE = 8
NX = 512
NY = 128
NZ = 128
BR_DEV = 64
N_SPACE = 32
N_SUB = 8


def draw_tile_count(key, part):
    counts = jax.random.randint(key, (N_SPACE, N_SUB, N_SPACE, N_SUB, TPD), SLOTS // 4, SLOTS + 1)
    return counts.astype(jnp.int32).at[0, 0, 0, 0, 0].set(SLOTS)


def with_ends(values, rng, smallest, largest):
    place = [jax.random.randint(jax.random.fold_in(rng, axis), (), 0, length) for axis, length in enumerate(values.shape)]
    widest = values.shape.index(max(values.shape))
    next_to = place[:widest] + [(place[widest] + 1) % values.shape[widest]] + place[widest + 1:]
    return values.at[tuple(place)].set(smallest).at[tuple(next_to)].set(largest)


def steps_of(rng, dims, shards, smallest, high):
    factor_of, own = 1.0, jax.random.fold_in(rng, 6)
    for axis_at, shards_of in shards:
        heights = jnp.exp(jax.random.uniform(jax.random.fold_in(own, axis_at), (shards_of,), jnp.float32, smallest / len(shards), high / len(shards)))
        factor_of = factor_of * jnp.repeat(heights, dims[axis_at] // shards_of).reshape([-1 if axis == axis_at else 1 for axis in range(len(dims))])
    return factor_of


def centred(own_key, extent, width, most, pieces=(), held_as=jnp.bfloat16):
    gain = steps_of(own_key, extent, pieces, -0.22, 0.18) if pieces else 1.0
    values = jax.random.normal(own_key, extent, jnp.float32) * width * gain
    return jnp.minimum(jnp.maximum(values, -most), most).astype(held_as)


def setup_inputs(seed: int = 0) -> dict:
    keys = jax.random.split(jax.random.key(seed), 6)
    offsets = jnp.clip(0.5 + 7.0 * jax.random.uniform(keys[0], (N_SPACE, N_SUB, N_SPACE, N_SUB, TPD, 3, SLOTS), jnp.float32) ** steps_of(keys[0], (N_SPACE, N_SUB, N_SPACE, N_SUB, TPD, 3, SLOTS), ((0, 32), (1, 8)), -0.2, 0.2), 0.5, 7.5)
    normals = centred(keys[1], (N_SPACE, N_SUB, N_SPACE, N_SUB, TPD, 3, SLOTS), 1.0, 6.0, ((0, 32), (1, 8)), jnp.float32)
    density = jnp.clip(jnp.exp(math.log(3.0) - 2.3025851 * jax.random.uniform(keys[2], (N_SPACE, N_SUB, N_SPACE, N_SUB, TPD, SLOTS), jnp.float32) ** steps_of(keys[2], (N_SPACE, N_SUB, N_SPACE, N_SUB, TPD, SLOTS), ((0, 32), (1, 8)), -0.2, 0.2)), 0.3, 3.0)
    tile_brick = with_ends(jax.random.randint(keys[3], (N_SPACE, N_SUB, N_SPACE, N_SUB, TPD), 0, BR_DEV), jax.random.fold_in(keys[3], 1), 0, BR_DEV - 1).astype(jnp.int32)
    tile_count = draw_tile_count(jax.random.fold_in(keys[5], 71), 0)
    return {"offsets": offsets, "normals": normals, "density": density, "tile_brick": tile_brick, "tile_count": tile_count}


screen_weight = 0.05
relax_weight = 0.8


def splat_tiles(offsets_tile, samples_tile):
    tile_total = offsets_tile.shape[0]
    slot_total = offsets_tile.shape[2]
    centers = jnp.arange(BRICK, dtype=jnp.float32) + 0.5
    weights = jnp.maximum(0.0, 1.0 - jnp.abs(offsets_tile[:, :, None, :] - centers[None, None, :, None]))
    planar = (weights[:, 0, :, None, :] * weights[:, 1, None, :, :]).reshape(tile_total, BRICK * BRICK, slot_total)
    loaded = (samples_tile[:, :, None, :] * weights[:, 2][:, None, :, :]).reshape(tile_total, 4 * BRICK, slot_total)
    result = jnp.einsum("tas,tbs->tab", planar, loaded, precision=lax.Precision.HIGHEST)
    return result.reshape(tile_total, -1)


def to_grid(sums):
    shaped = sums.reshape(CX // BRICK, CY // BRICK, CZ // BRICK, BRICK, BRICK, 4, BRICK)
    return shaped.transpose(5, 0, 3, 1, 4, 2, 6).reshape(4, CX, CY, CZ)


def neighbours(padded):
    total = padded[2:, 1:-1, 1:-1] + padded[:-2, 1:-1, 1:-1]
    total = total + padded[1:-1, 2:, 1:-1] + padded[1:-1, :-2, 1:-1]
    return total + padded[1:-1, 1:-1, 2:] + padded[1:-1, 1:-1, :-2]


def operate(field, screen, level_index):
    return (6.0 * field - neighbours(jnp.pad(field, 1))) * (0.25 ** level_index) + screen * field


def sweep(field, forcing, screen, diagonal, level_index):
    return field + relax_weight * (forcing - operate(field, screen, level_index)) / diagonal


def restrict(field):
    sx, sy, sz = field.shape
    return field.reshape(sx // 2, 2, sy // 2, 2, sz // 2, 2).mean(axis=(1, 3, 5))


def prolong(field):
    return jnp.repeat(jnp.repeat(jnp.repeat(field, 2, axis=0), 2, axis=1), 2, axis=2)


def vcycle(forcing, level_index, screens):
    screen = screens[level_index]
    diagonal = 6.0 * (0.25 ** level_index) + screen
    field = relax_weight * forcing / diagonal
    if level_index == LEVELS - 1:
        for sweep_index in range(COARSE - 1):
            field = sweep(field, forcing, screen, diagonal, level_index)
        return field
    for sweep_index in range(SWEEPS - 1):
        field = sweep(field, forcing, screen, diagonal, level_index)
    residual = forcing - operate(field, screen, level_index)
    correction = vcycle(restrict(residual), level_index + 1, screens)
    field = field + prolong(correction)
    for sweep_index in range(SWEEPS):
        field = sweep(field, forcing, screen, diagonal, level_index)
    return field


def reference(offsets, normals, density, tile_brick, tile_count):
    brick_total = (CX // BRICK) * (CY // BRICK) * (CZ // BRICK)

    def pick(array, target_space, target_sub):
        first = lax.dynamic_index_in_dim(array, target_space, 2, keepdims=False)
        return lax.dynamic_index_in_dim(first, target_sub, 2, keepdims=False)

    def one_target(target):
        target_space = target // N_SUB
        target_sub = target % N_SUB
        offsets_here = pick(offsets, target_space, target_sub).reshape(-1, 3, SLOTS)
        normals_here = pick(normals, target_space, target_sub).reshape(-1, 3, SLOTS)
        density_here = pick(density, target_space, target_sub).reshape(-1, 1, SLOTS)
        counts_here = pick(tile_count, target_space, target_sub).reshape(-1)
        bricks_here = pick(tile_brick, target_space, target_sub).reshape(-1)
        live_slots = (jnp.arange(SLOTS, dtype=jnp.int32)[None, :] < counts_here[:, None]).astype(jnp.float32)
        samples = jnp.concatenate([normals_here, density_here], axis=1) * live_slots[:, None, :]
        partials = splat_tiles(offsets_here, samples)
        onehot = (bricks_here[None, :] == jnp.arange(brick_total, dtype=jnp.int32)[:, None]).astype(jnp.float32)
        sums = jnp.dot(onehot, partials, precision=lax.Precision.HIGHEST, preferred_element_type=jnp.float32)
        return to_grid(sums)

    blocks = lax.map(one_target, jnp.arange(N_SPACE * N_SUB, dtype=jnp.int32))
    grid = blocks.reshape(N_SPACE, N_SUB, 4, CX, CY, CZ).transpose(2, 0, 3, 1, 4, 5).reshape(4, NX, NY, NZ)
    density_field = grid[3]
    padded_x = jnp.pad(grid[0], ((1, 1), (0, 0), (0, 0)))
    padded_y = jnp.pad(grid[1], ((0, 0), (1, 1), (0, 0)))
    padded_z = jnp.pad(grid[2], ((0, 0), (0, 0), (1, 1)))
    change = (padded_x[2:] - padded_x[:-2]) + (padded_y[:, 2:] - padded_y[:, :-2])
    change = change + (padded_z[:, :, 2:] - padded_z[:, :, :-2])
    forcing = -0.5 * change
    screens = []
    rho_level = density_field
    for level_index in range(LEVELS):
        screens.append(screen_weight * rho_level)
        rho_level = restrict(rho_level) if level_index < LEVELS - 1 else rho_level
    indicator = vcycle(forcing, 0, screens)
    return indicator, density_field
```

```python
import jax
import jax.numpy as jnp
from jax import lax
from jax.sharding import PartitionSpec as P

BRICK = 8
CX = 16
CY = 16
CZ = 128
LEVELS = 4
SWEEPS = 2
COARSE = 8

screen_weight = 0.05
relax_weight = 0.8

HALO0 = 4
HALO1 = 4


def exchange(x, width, dim_x, dim_y):
    for axis, dim in (("space", dim_x), ("sub", dim_y)):
        devices = lax.axis_size(axis)
        length = x.shape[dim]
        up = [(i, i + 1) for i in range(devices - 1)]
        down = [(j, i) for i, j in up]
        last = lax.slice_in_dim(x, length - width, length, axis=dim)
        first = lax.slice_in_dim(x, 0, width, axis=dim)
        before = lax.ppermute(last, axis, up)
        after = lax.ppermute(first, axis, down)
        x = jnp.concatenate([before, x, after], axis=dim)
    return x


def crop(x, h_from, h_to):
    d = h_from - h_to
    if d == 0:
        return x
    return x[d:-d, d:-d]


def inside_mask(nx, ny, nz, halo):
    dev_x = lax.axis_index("space")
    dev_y = lax.axis_index("sub")
    total_x = lax.axis_size("space") * nx
    total_y = lax.axis_size("sub") * ny
    gx = lax.broadcasted_iota(jnp.int32, (nx + 2 * halo, ny + 2 * halo, nz), 0) + dev_x * nx - halo
    gy = lax.broadcasted_iota(jnp.int32, (nx + 2 * halo, ny + 2 * halo, nz), 1) + dev_y * ny - halo
    ok = (gx >= 0) & (gx < total_x) & (gy >= 0) & (gy < total_y)
    return ok.astype(jnp.float32)


def operate_ext(u, screen_c, scale):
    c = u[1:-1, 1:-1, :]
    zp = jnp.pad(c, ((0, 0), (0, 0), (1, 1)))
    total = u[2:, 1:-1] + u[:-2, 1:-1]
    total = total + u[1:-1, 2:] + u[1:-1, :-2]
    total = total + zp[:, :, 2:] + zp[:, :, :-2]
    return (6.0 * c - total) * scale + screen_c * c


def sweep_ext(u, h, f, screen, diag, mask, scale):
    fc, sc, dc = crop(f, h, h - 1), crop(screen, h, h - 1), crop(diag, h, h - 1)
    new = crop(u, h, h - 1) + relax_weight * (fc - operate_ext(u, sc, scale)) / dc
    return new * crop(mask, h, h - 1)


def restrict(field):
    sx, sy, sz = field.shape
    return field.reshape(sx // 2, 2, sy // 2, 2, sz // 2, 2).mean(axis=(1, 3, 5))


def prolong(field):
    return jnp.repeat(jnp.repeat(jnp.repeat(field, 2, axis=0), 2, axis=1), 2, axis=2)


def neighbours(padded):
    total = padded[2:, 1:-1, 1:-1] + padded[:-2, 1:-1, 1:-1]
    total = total + padded[1:-1, 2:, 1:-1] + padded[1:-1, :-2, 1:-1]
    return total + padded[1:-1, 1:-1, 2:] + padded[1:-1, 1:-1, :-2]


def operate(field, screen, level_index):
    return (6.0 * field - neighbours(jnp.pad(field, 1))) * (0.25**level_index) + screen * field


def sweep(field, forcing, screen, diagonal, level_index):
    return field + relax_weight * (forcing - operate(field, screen, level_index)) / diagonal


def vcycle_global(forcing, level_index, screens):
    screen = screens[level_index]
    diagonal = 6.0 * (0.25**level_index) + screen
    field = relax_weight * forcing / diagonal
    if level_index == LEVELS - 1:
        for _ in range(COARSE - 1):
            field = sweep(field, forcing, screen, diagonal, level_index)
        return field
    for _ in range(SWEEPS - 1):
        field = sweep(field, forcing, screen, diagonal, level_index)
    residual = forcing - operate(field, screen, level_index)
    correction = vcycle_global(restrict(residual), level_index + 1, screens)
    field = field + prolong(correction)
    for _ in range(SWEEPS):
        field = sweep(field, forcing, screen, diagonal, level_index)
    return field


def splat(packed):
    tiles, _, slots = packed.shape
    offsets = packed[:, 0:3, :]
    samples = packed[:, 3:7, :]
    bricks = packed[:, 7, 0].astype(jnp.int32)
    centers = jnp.arange(BRICK, dtype=jnp.float32) + 0.5
    weights = jnp.maximum(0.0, 1.0 - jnp.abs(offsets[:, :, None, :] - centers[None, None, :, None]))
    planar = (weights[:, 0, :, None, :] * weights[:, 1, None, :, :]).reshape(
        tiles, BRICK * BRICK, slots
    )
    loaded = (samples[:, :, None, :] * weights[:, 2][:, None, :, :]).reshape(
        tiles, 4 * BRICK, slots
    )
    partials = jnp.einsum("tas,tbs->tab", planar, loaded, precision=lax.Precision.HIGHEST)
    partials = partials.reshape(tiles, -1)
    brick_total = CX // BRICK * (CY // BRICK) * (CZ // BRICK)
    onehot = (bricks[None, :] == jnp.arange(brick_total, dtype=jnp.int32)[:, None]).astype(
        jnp.float32
    )
    return jnp.dot(
        onehot, partials, precision=lax.Precision.HIGHEST, preferred_element_type=jnp.float32
    )


def to_grid(sums):
    shaped = sums.reshape(CX // BRICK, CY // BRICK, CZ // BRICK, BRICK, BRICK, 4, BRICK)
    return shaped.transpose(5, 0, 3, 1, 4, 2, 6).reshape(4, CX, CY, CZ)


def on_device(offsets, normals, density, tile_brick, tile_count):
    space_count = lax.axis_size("space")
    sub_count = lax.axis_size("sub")
    devices = space_count * sub_count
    tiles_each = offsets.shape[4]
    slot_total = offsets.shape[6]

    slot_numbers = lax.broadcasted_iota(jnp.int32, (devices, tiles_each, 1, slot_total), 3)
    live = (slot_numbers < tile_count.reshape(devices, tiles_each, 1, 1)).astype(jnp.float32)
    samples = jnp.concatenate(
        [
            normals.reshape(devices, tiles_each, 3, slot_total),
            density.reshape(devices, tiles_each, 1, slot_total),
        ],
        axis=2,
    ) * live
    brick_row = jnp.broadcast_to(
        tile_brick.reshape(devices, tiles_each, 1, 1).astype(jnp.float32),
        (devices, tiles_each, 1, slot_total),
    )
    packed = jnp.concatenate(
        [offsets.reshape(devices, tiles_each, 3, slot_total), samples, brick_row], axis=2
    )
    received = lax.all_to_all(packed, ("space", "sub"), 0, 0, tiled=True)
    sums = splat(received.reshape(devices * tiles_each, 8, slot_total))
    grid = to_grid(sums)
    density_field = grid[3]

    h0 = HALO0
    g = exchange(grid, h0, 1, 2)
    vx, vy, vz, rho0 = g[0], g[1], g[2], g[3]
    mask0 = inside_mask(CX, CY, CZ, h0)
    hf = h0 - 1
    vzc = jnp.pad(crop(vz, h0, hf), ((0, 0), (0, 0), (1, 1)))
    change = vx[2:, 1:-1] - vx[:-2, 1:-1] + (vy[1:-1, 2:] - vy[1:-1, :-2])
    change = change + (vzc[:, :, 2:] - vzc[:, :, :-2])
    m0 = crop(mask0, h0, hf)
    f0 = -0.5 * change * m0
    screen0 = screen_weight * crop(rho0, h0, hf)
    diag0 = 6.0 + screen0
    u = relax_weight * f0 / diag0 * m0
    u = sweep_ext(u, hf, f0, screen0, diag0, m0, 1.0)
    hu0 = hf - 1
    residual0 = crop(f0, hf, 0) - operate_ext(
        crop(u, hu0, 1), crop(screen0, hf, 0), 1.0
    )

    h1 = HALO1
    f1 = restrict(residual0)
    rho1 = restrict(density_field)
    nx1, ny1, nz1 = f1.shape
    both = exchange(jnp.stack([f1, rho1]), h1, 1, 2)
    f1e, rho1e = both[0], both[1]
    mask1 = inside_mask(nx1, ny1, nz1, h1)
    scale1 = 0.25
    screen1 = screen_weight * rho1e
    diag1 = 6.0 * scale1 + screen1
    u1 = relax_weight * f1e / diag1 * mask1
    u1 = sweep_ext(u1, h1, f1e, screen1, diag1, mask1, scale1)
    hu1 = h1 - 1
    residual1 = crop(f1e, h1, 0) - operate_ext(crop(u1, hu1, 1), crop(screen1, h1, 0), scale1)

    f2 = restrict(residual1)
    rho2 = restrict(rho1)
    nx2, ny2, nz2 = f2.shape

    def gather(x):
        every = lax.all_gather(x, ("space", "sub"), axis=0, tiled=False)
        every = every.reshape(space_count, sub_count, nx2, ny2, nz2)
        return every.transpose(0, 2, 1, 3, 4).reshape(space_count * nx2, sub_count * ny2, nz2)

    rho2g = gather(rho2)
    f2g = gather(f2)
    rho3g = restrict(rho2g)
    screens = [None, None, screen_weight * rho2g, screen_weight * rho3g]
    c2g = vcycle_global(f2g, 2, screens)
    hc2 = (hu1 + 1) // 2
    c2p = jnp.pad(c2g, ((hc2, hc2), (hc2, hc2), (0, 0)))
    c2 = lax.dynamic_slice(
        c2p,
        (lax.axis_index("space") * nx2, lax.axis_index("sub") * ny2, 0),
        (nx2 + 2 * hc2, ny2 + 2 * hc2, nz2),
    )

    u1 = u1 + crop(prolong(c2), 2 * hc2, hu1)
    hcur = hu1
    while hcur > 1:
        u1 = sweep_ext(
            u1,
            hcur,
            crop(f1e, h1, hcur),
            crop(screen1, h1, hcur),
            crop(diag1, h1, hcur),
            crop(mask1, h1, hcur),
            scale1,
        )
        hcur -= 1
    c1 = u1

    u = u + crop(prolong(c1), 2, hu0)
    hcur = hu0
    for _ in range(SWEEPS):
        u = sweep_ext(
            u,
            hcur,
            crop(f0, hf, hcur),
            crop(screen0, hf, hcur),
            crop(diag0, hf, hcur),
            crop(m0, hf, hcur),
            1.0,
        )
        hcur -= 1
    indicator = crop(u, hcur, 0)
    return (indicator, density_field)


def solution(mesh):
    placed = (
        P("space", "sub", None, None, None, None, None),
        P("space", "sub", None, None, None, None, None),
        P("space", "sub", None, None, None, None),
        P("space", "sub", None, None, None),
        P("space", "sub", None, None, None),
    )
    return jax.shard_map(
        on_device,
        mesh=mesh,
        in_specs=placed,
        out_specs=(P("space", "sub", None), P("space", "sub", None)),
        check_vma=False,
    )
```

```python
import jax
import jax.numpy as jnp
from jax import lax
from jax.sharding import PartitionSpec as P

BRICK = 8
CX = 16
CY = 16
CZ = 128
LEVELS = 4
SWEEPS = 2
COARSE = 8

screen_weight = 0.05
relax_weight = 0.8

HALO0 = 4
HALO1 = 4


def exchange(x, width, dim_x, dim_y):
    for axis, dim in (("space", dim_x), ("sub", dim_y)):
        devices = lax.axis_size(axis)
        length = x.shape[dim]
        up = [(i, i + 1) for i in range(devices - 1)]
        down = [(j, i) for i, j in up]
        last = lax.slice_in_dim(x, length - width, length, axis=dim)
        first = lax.slice_in_dim(x, 0, width, axis=dim)
        before = lax.ppermute(last, axis, up)
        after = lax.ppermute(first, axis, down)
        x = jnp.concatenate([before, x, after], axis=dim)
    return x


def crop(x, h_from, h_to):
    d = h_from - h_to
    if d == 0:
        return x
    return x[d:-d, d:-d]


def inside_mask(nx, ny, nz, halo):
    dev_x = lax.axis_index("space")
    dev_y = lax.axis_index("sub")
    total_x = lax.axis_size("space") * nx
    total_y = lax.axis_size("sub") * ny
    gx = lax.broadcasted_iota(jnp.int32, (nx + 2 * halo, ny + 2 * halo, nz), 0) + dev_x * nx - halo
    gy = lax.broadcasted_iota(jnp.int32, (nx + 2 * halo, ny + 2 * halo, nz), 1) + dev_y * ny - halo
    ok = (gx >= 0) & (gx < total_x) & (gy >= 0) & (gy < total_y)
    return ok.astype(jnp.float32)


def operate_ext(u, screen_c, scale):
    c = u[1:-1, 1:-1, :]
    zp = jnp.pad(c, ((0, 0), (0, 0), (1, 1)))
    total = u[2:, 1:-1] + u[:-2, 1:-1]
    total = total + u[1:-1, 2:] + u[1:-1, :-2]
    total = total + zp[:, :, 2:] + zp[:, :, :-2]
    return (6.0 * c - total) * scale + screen_c * c


def sweep_ext(u, h, f, screen, diag, mask, scale):
    fc, sc, dc = crop(f, h, h - 1), crop(screen, h, h - 1), crop(diag, h, h - 1)
    new = crop(u, h, h - 1) + relax_weight * (fc - operate_ext(u, sc, scale)) / dc
    return new * crop(mask, h, h - 1)


def pair_matrix(n):
    rows = lax.broadcasted_iota(jnp.int32, (n, n // 2), 0) // 2
    cols = lax.broadcasted_iota(jnp.int32, (n, n // 2), 1)
    return (rows == cols).astype(jnp.float32)


def restrict(field):
    sx, sy, sz = field.shape
    zs = jnp.dot(
        field.reshape(sx * sy, sz), pair_matrix(sz), precision=lax.Precision.HIGHEST
    ).reshape(sx, sy, sz // 2)
    xs = zs.reshape(sx // 2, 2, sy, sz // 2).sum(axis=1)
    ys = xs.reshape(sx // 2, sy // 2, 2, sz // 2).sum(axis=2)
    return ys * 0.125


def prolong(field):
    sx, sy, sz = field.shape
    zs = jnp.dot(
        field.reshape(sx * sy, sz), pair_matrix(2 * sz).T, precision=lax.Precision.HIGHEST
    ).reshape(sx, sy, 2 * sz)
    return jnp.repeat(jnp.repeat(zs, 2, axis=0), 2, axis=1)


def neighbours(padded):
    total = padded[2:, 1:-1, 1:-1] + padded[:-2, 1:-1, 1:-1]
    total = total + padded[1:-1, 2:, 1:-1] + padded[1:-1, :-2, 1:-1]
    return total + padded[1:-1, 1:-1, 2:] + padded[1:-1, 1:-1, :-2]


def operate(field, screen, level_index):
    return (6.0 * field - neighbours(jnp.pad(field, 1))) * (0.25**level_index) + screen * field


def sweep(field, forcing, screen, diagonal, level_index):
    return field + relax_weight * (forcing - operate(field, screen, level_index)) / diagonal


def vcycle_global(forcing, level_index, screens):
    screen = screens[level_index]
    diagonal = 6.0 * (0.25**level_index) + screen
    field = relax_weight * forcing / diagonal
    if level_index == LEVELS - 1:
        for _ in range(COARSE - 1):
            field = sweep(field, forcing, screen, diagonal, level_index)
        return field
    for _ in range(SWEEPS - 1):
        field = sweep(field, forcing, screen, diagonal, level_index)
    residual = forcing - operate(field, screen, level_index)
    correction = vcycle_global(restrict(residual), level_index + 1, screens)
    field = field + prolong(correction)
    for _ in range(SWEEPS):
        field = sweep(field, forcing, screen, diagonal, level_index)
    return field


def splat(packed):
    tiles, _, slots = packed.shape
    offsets = packed[:, 0:3, :]
    samples = packed[:, 3:7, :]
    centers = jnp.arange(BRICK, dtype=jnp.float32) + 0.5
    weights = jnp.maximum(0.0, 1.0 - jnp.abs(offsets[:, :, None, :] - centers[None, None, :, None]))
    planar = (weights[:, 0, :, None, :] * weights[:, 1, None, :, :]).reshape(
        tiles, BRICK * BRICK, slots
    )
    loaded = (samples[:, :, None, :] * weights[:, 2][:, None, :, :]).reshape(
        tiles, 4 * BRICK, slots
    )
    partials = jnp.einsum("tas,tbs->tab", planar, loaded, precision=lax.Precision.HIGH)
    brick_total = CX // BRICK * (CY // BRICK) * (CZ // BRICK)
    brick_row = packed[:, 7, :brick_total]
    numbers = lax.broadcasted_iota(jnp.float32, (tiles, brick_total), 1)
    onehot = (brick_row == numbers).astype(jnp.float32)
    sums = jnp.einsum("tk,tab->kab", onehot, partials, precision=lax.Precision.HIGHEST)
    return sums.reshape(brick_total, -1)


def to_grid(sums):
    shaped = sums.reshape(CX // BRICK, CY // BRICK, CZ // BRICK, BRICK, BRICK, 4, BRICK)
    return shaped.transpose(5, 0, 3, 1, 4, 2, 6).reshape(4, CX, CY, CZ)


def on_device(offsets, normals, density, tile_brick, tile_count):
    space_count = lax.axis_size("space")
    sub_count = lax.axis_size("sub")
    devices = space_count * sub_count
    tiles_each = offsets.shape[4]
    slot_total = offsets.shape[6]

    slot_numbers = lax.broadcasted_iota(jnp.int32, (devices, tiles_each, 1, slot_total), 3)
    live = (slot_numbers < tile_count.reshape(devices, tiles_each, 1, 1)).astype(jnp.float32)
    samples = jnp.concatenate(
        [
            normals.reshape(devices, tiles_each, 3, slot_total),
            density.reshape(devices, tiles_each, 1, slot_total),
        ],
        axis=2,
    ) * live
    brick_row = jnp.broadcast_to(
        tile_brick.reshape(devices, tiles_each, 1, 1).astype(jnp.float32),
        (devices, tiles_each, 1, slot_total),
    )
    packed = jnp.concatenate(
        [offsets.reshape(devices, tiles_each, 3, slot_total), samples, brick_row], axis=2
    )
    received = lax.all_to_all(packed, ("space", "sub"), 0, 0, tiled=True)
    sums = splat(received.reshape(devices * tiles_each, 8, slot_total))
    grid = to_grid(sums)
    density_field = grid[3]

    h0 = HALO0
    g = exchange(grid, h0, 1, 2)
    vx, vy, vz, rho0 = g[0], g[1], g[2], g[3]
    mask0 = inside_mask(CX, CY, CZ, h0)
    hf = h0 - 1
    vzc = jnp.pad(crop(vz, h0, hf), ((0, 0), (0, 0), (1, 1)))
    change = vx[2:, 1:-1] - vx[:-2, 1:-1] + (vy[1:-1, 2:] - vy[1:-1, :-2])
    change = change + (vzc[:, :, 2:] - vzc[:, :, :-2])
    m0 = crop(mask0, h0, hf)
    f0 = -0.5 * change * m0
    screen0 = screen_weight * crop(rho0, h0, hf)
    diag0 = 6.0 + screen0
    u = relax_weight * f0 / diag0 * m0
    u = sweep_ext(u, hf, f0, screen0, diag0, m0, 1.0)
    hu0 = hf - 1
    residual0 = crop(f0, hf, 0) - operate_ext(
        crop(u, hu0, 1), crop(screen0, hf, 0), 1.0
    )

    h1 = HALO1
    f1 = restrict(residual0)
    rho1 = restrict(density_field)
    nx1, ny1, nz1 = f1.shape
    both = exchange(jnp.stack([f1, rho1]), h1, 1, 2)
    f1e, rho1e = both[0], both[1]
    mask1 = inside_mask(nx1, ny1, nz1, h1)
    scale1 = 0.25
    screen1 = screen_weight * rho1e
    diag1 = 6.0 * scale1 + screen1
    u1 = relax_weight * f1e / diag1 * mask1
    u1 = sweep_ext(u1, h1, f1e, screen1, diag1, mask1, scale1)
    hu1 = h1 - 1
    residual1 = crop(f1e, h1, 0) - operate_ext(crop(u1, hu1, 1), crop(screen1, h1, 0), scale1)

    f2 = restrict(residual1)
    rho2 = restrict(rho1)
    nx2, ny2, nz2 = f2.shape

    both2 = jnp.stack([f2, rho2]).reshape(-1, 128)
    every = lax.all_gather(both2, ("space", "sub"), axis=0, tiled=False)
    every = every.reshape(space_count, sub_count, 2, nx2, ny2, nz2)
    every = every.transpose(2, 0, 3, 1, 4, 5).reshape(2, space_count * nx2, sub_count * ny2, nz2)
    f2g, rho2g = every[0], every[1]
    rho3g = restrict(rho2g)
    screens = [None, None, screen_weight * rho2g, screen_weight * rho3g]
    c2g = vcycle_global(f2g, 2, screens)
    hc2 = (hu1 + 1) // 2
    c2p = jnp.pad(c2g, ((hc2, hc2), (hc2, hc2), (0, 0)))
    c2 = lax.dynamic_slice(
        c2p,
        (lax.axis_index("space") * nx2, lax.axis_index("sub") * ny2, 0),
        (nx2 + 2 * hc2, ny2 + 2 * hc2, nz2),
    )

    u1 = u1 + crop(prolong(c2), 2 * hc2, hu1)
    hcur = hu1
    while hcur > 1:
        u1 = sweep_ext(
            u1,
            hcur,
            crop(f1e, h1, hcur),
            crop(screen1, h1, hcur),
            crop(diag1, h1, hcur),
            crop(mask1, h1, hcur),
            scale1,
        )
        hcur -= 1
    c1 = u1

    u = u + crop(prolong(c1), 2, hu0)
    hcur = hu0
    for _ in range(SWEEPS):
        u = sweep_ext(
            u,
            hcur,
            crop(f0, hf, hcur),
            crop(screen0, hf, hcur),
            crop(diag0, hf, hcur),
            crop(m0, hf, hcur),
            1.0,
        )
        hcur -= 1
    indicator = crop(u, hcur, 0)
    return (indicator, density_field)


def solution(mesh):
    placed = (
        P("space", "sub", None, None, None, None, None),
        P("space", "sub", None, None, None, None, None),
        P("space", "sub", None, None, None, None),
        P("space", "sub", None, None, None),
        P("space", "sub", None, None, None),
    )
    return jax.shard_map(
        on_device,
        mesh=mesh,
        in_specs=placed,
        out_specs=(P("space", "sub", None), P("space", "sub", None)),
        check_vma=False,
    )
```

```python
import jax
import jax.numpy as jnp
from jax import lax
from jax.sharding import PartitionSpec as P

BRICK = 8
CX = 16
CY = 16
CZ = 128
LEVELS = 4
SWEEPS = 2
COARSE = 8

screen_weight = 0.05
relax_weight = 0.8

HALO0 = 4
HALO1 = 4


def exchange(x, width, dim_x, dim_y):
    for axis, dim in (("space", dim_x), ("sub", dim_y)):
        devices = lax.axis_size(axis)
        length = x.shape[dim]
        up = [(i, i + 1) for i in range(devices - 1)]
        down = [(j, i) for i, j in up]
        last = lax.slice_in_dim(x, length - width, length, axis=dim)
        first = lax.slice_in_dim(x, 0, width, axis=dim)
        before = lax.ppermute(last, axis, up)
        after = lax.ppermute(first, axis, down)
        x = jnp.concatenate([before, x, after], axis=dim)
    return x


def crop(x, h_from, h_to):
    d = h_from - h_to
    if d == 0:
        return x
    return x[d:-d, d:-d]


def inside_mask(nx, ny, nz, halo):
    dev_x = lax.axis_index("space")
    dev_y = lax.axis_index("sub")
    total_x = lax.axis_size("space") * nx
    total_y = lax.axis_size("sub") * ny
    gx = lax.broadcasted_iota(jnp.int32, (nx + 2 * halo, ny + 2 * halo, nz), 0) + dev_x * nx - halo
    gy = lax.broadcasted_iota(jnp.int32, (nx + 2 * halo, ny + 2 * halo, nz), 1) + dev_y * ny - halo
    ok = (gx >= 0) & (gx < total_x) & (gy >= 0) & (gy < total_y)
    return ok.astype(jnp.float32)


def operate_ext(u, screen_c, scale):
    c = u[1:-1, 1:-1, :]
    zp = jnp.pad(c, ((0, 0), (0, 0), (1, 1)))
    total = u[2:, 1:-1] + u[:-2, 1:-1]
    total = total + u[1:-1, 2:] + u[1:-1, :-2]
    total = total + zp[:, :, 2:] + zp[:, :, :-2]
    return (6.0 * c - total) * scale + screen_c * c


def sweep_ext(u, h, f, screen, diag, mask, scale):
    fc, sc, dc = crop(f, h, h - 1), crop(screen, h, h - 1), crop(diag, h, h - 1)
    new = crop(u, h, h - 1) + relax_weight * (fc - operate_ext(u, sc, scale)) / dc
    return new * crop(mask, h, h - 1)


def pair_matrix(n):
    rows = lax.broadcasted_iota(jnp.int32, (n, n // 2), 0) // 2
    cols = lax.broadcasted_iota(jnp.int32, (n, n // 2), 1)
    return (rows == cols).astype(jnp.float32)


def restrict(field):
    sx, sy, sz = field.shape
    zs = jnp.dot(
        field.reshape(sx * sy, sz), pair_matrix(sz), precision=lax.Precision.HIGHEST
    ).reshape(sx, sy, sz // 2)
    xs = zs.reshape(sx // 2, 2, sy, sz // 2).sum(axis=1)
    ys = xs.reshape(sx // 2, sy // 2, 2, sz // 2).sum(axis=2)
    return ys * 0.125


def prolong(field):
    sx, sy, sz = field.shape
    zs = jnp.dot(
        field.reshape(sx * sy, sz), pair_matrix(2 * sz).T, precision=lax.Precision.HIGHEST
    ).reshape(sx, sy, 2 * sz)
    return jnp.repeat(jnp.repeat(zs, 2, axis=0), 2, axis=1)


def neighbours(padded):
    total = padded[2:, 1:-1, 1:-1] + padded[:-2, 1:-1, 1:-1]
    total = total + padded[1:-1, 2:, 1:-1] + padded[1:-1, :-2, 1:-1]
    return total + padded[1:-1, 1:-1, 2:] + padded[1:-1, 1:-1, :-2]


def operate(field, screen, level_index):
    return (6.0 * field - neighbours(jnp.pad(field, 1))) * (0.25**level_index) + screen * field


def sweep(field, forcing, screen, diagonal, level_index):
    return field + relax_weight * (forcing - operate(field, screen, level_index)) / diagonal


def vcycle_global(forcing, level_index, screens):
    screen = screens[level_index]
    diagonal = 6.0 * (0.25**level_index) + screen
    field = relax_weight * forcing / diagonal
    if level_index == LEVELS - 1:
        for _ in range(COARSE - 1):
            field = sweep(field, forcing, screen, diagonal, level_index)
        return field
    for _ in range(SWEEPS - 1):
        field = sweep(field, forcing, screen, diagonal, level_index)
    residual = forcing - operate(field, screen, level_index)
    correction = vcycle_global(restrict(residual), level_index + 1, screens)
    field = field + prolong(correction)
    for _ in range(SWEEPS):
        field = sweep(field, forcing, screen, diagonal, level_index)
    return field


def splat(packed):
    tiles, _, slots = packed.shape
    offsets = packed[:, 0:3, :]
    samples = packed[:, 3:7, :]
    centers = jnp.arange(BRICK, dtype=jnp.float32) + 0.5
    weights = jnp.maximum(0.0, 1.0 - jnp.abs(offsets[:, :, None, :] - centers[None, None, :, None]))
    planar = (weights[:, 0, :, None, :] * weights[:, 1, None, :, :]).reshape(
        tiles, BRICK * BRICK, slots
    )
    loaded = (samples[:, :, None, :] * weights[:, 2][:, None, :, :]).reshape(
        tiles, 4 * BRICK, slots
    )
    partials = jnp.einsum("tas,tbs->tab", planar, loaded, precision=lax.Precision.HIGH)
    brick_total = CX // BRICK * (CY // BRICK) * (CZ // BRICK)
    brick_row = packed[:, 7, :brick_total]
    numbers = lax.broadcasted_iota(jnp.float32, (tiles, brick_total), 1)
    onehot = (brick_row == numbers).astype(jnp.float32)
    sums = jnp.einsum("tk,tab->kab", onehot, partials, precision=lax.Precision.HIGHEST)
    return sums.reshape(brick_total, -1)


def gather_all(block, space_count, sub_count):
    channels, nx, ny, nz = block.shape
    devices = space_count * sub_count
    flat = block.reshape(1, -1, 128)
    sent = jnp.broadcast_to(flat, (devices,) + flat.shape[1:])
    every = lax.all_to_all(sent, ("space", "sub"), 0, 0, tiled=True)
    every = every.reshape(space_count, sub_count, channels, nx, ny, nz)
    every = every.transpose(2, 0, 3, 1, 4, 5)
    return every.reshape(channels, space_count * nx, sub_count * ny, nz)


def to_grid(sums):
    shaped = sums.reshape(CX // BRICK, CY // BRICK, CZ // BRICK, BRICK, BRICK, 4, BRICK)
    return shaped.transpose(5, 0, 3, 1, 4, 2, 6).reshape(4, CX, CY, CZ)


def on_device(offsets, normals, density, tile_brick, tile_count):
    space_count = lax.axis_size("space")
    sub_count = lax.axis_size("sub")
    devices = space_count * sub_count
    tiles_each = offsets.shape[4]
    slot_total = offsets.shape[6]

    slot_numbers = lax.broadcasted_iota(jnp.int32, (devices, tiles_each, 1, slot_total), 3)
    live = (slot_numbers < tile_count.reshape(devices, tiles_each, 1, 1)).astype(jnp.float32)
    samples = jnp.concatenate(
        [
            normals.reshape(devices, tiles_each, 3, slot_total),
            density.reshape(devices, tiles_each, 1, slot_total),
        ],
        axis=2,
    ) * live
    brick_row = jnp.broadcast_to(
        tile_brick.reshape(devices, tiles_each, 1, 1).astype(jnp.float32),
        (devices, tiles_each, 1, slot_total),
    )
    packed = jnp.concatenate(
        [offsets.reshape(devices, tiles_each, 3, slot_total), samples, brick_row], axis=2
    )
    received = lax.all_to_all(packed, ("space", "sub"), 0, 0, tiled=True)
    sums = splat(received.reshape(devices * tiles_each, 8, slot_total))
    grid = to_grid(sums)
    density_field = grid[3]

    h0 = HALO0
    g = exchange(grid, h0, 1, 2)
    vx, vy, vz, rho0 = g[0], g[1], g[2], g[3]
    mask0 = inside_mask(CX, CY, CZ, h0)
    hf = h0 - 1
    vzc = jnp.pad(crop(vz, h0, hf), ((0, 0), (0, 0), (1, 1)))
    change = vx[2:, 1:-1] - vx[:-2, 1:-1] + (vy[1:-1, 2:] - vy[1:-1, :-2])
    change = change + (vzc[:, :, 2:] - vzc[:, :, :-2])
    m0 = crop(mask0, h0, hf)
    f0 = -0.5 * change * m0
    screen0 = screen_weight * crop(rho0, h0, hf)
    diag0 = 6.0 + screen0
    u = relax_weight * f0 / diag0 * m0
    u = sweep_ext(u, hf, f0, screen0, diag0, m0, 1.0)
    hu0 = hf - 1
    residual0 = crop(f0, hf, 0) - operate_ext(
        crop(u, hu0, 1), crop(screen0, hf, 0), 1.0
    )

    h1 = HALO1
    f1 = restrict(residual0)
    rho1 = restrict(density_field)
    nx1, ny1, nz1 = f1.shape
    both = exchange(jnp.stack([f1, rho1]), h1, 1, 2)
    f1e, rho1e = both[0], both[1]
    mask1 = inside_mask(nx1, ny1, nz1, h1)
    scale1 = 0.25
    screen1 = screen_weight * rho1e
    diag1 = 6.0 * scale1 + screen1
    u1 = relax_weight * f1e / diag1 * mask1
    u1 = sweep_ext(u1, h1, f1e, screen1, diag1, mask1, scale1)
    hu1 = h1 - 1
    residual1 = crop(f1e, h1, 0) - operate_ext(crop(u1, hu1, 1), crop(screen1, h1, 0), scale1)

    f2 = restrict(residual1)
    nx2, ny2, nz2 = f2.shape

    rho2 = restrict(rho1)
    both2 = gather_all(jnp.stack([f2, rho2]), space_count, sub_count)
    f2g, rho2g = both2[0], both2[1]
    rho3g = restrict(rho2g)
    screens = [None, None, screen_weight * rho2g, screen_weight * rho3g]
    c2g = vcycle_global(f2g, 2, screens)
    hc2 = (hu1 + 1) // 2
    c2p = jnp.pad(c2g, ((hc2, hc2), (hc2, hc2), (0, 0)))
    c2 = lax.dynamic_slice(
        c2p,
        (lax.axis_index("space") * nx2, lax.axis_index("sub") * ny2, 0),
        (nx2 + 2 * hc2, ny2 + 2 * hc2, nz2),
    )

    u1 = u1 + crop(prolong(c2), 2 * hc2, hu1)
    hcur = hu1
    while hcur > 1:
        u1 = sweep_ext(
            u1,
            hcur,
            crop(f1e, h1, hcur),
            crop(screen1, h1, hcur),
            crop(diag1, h1, hcur),
            crop(mask1, h1, hcur),
            scale1,
        )
        hcur -= 1
    c1 = u1

    u = u + crop(prolong(c1), 2, hu0)
    hcur = hu0
    for _ in range(SWEEPS):
        u = sweep_ext(
            u,
            hcur,
            crop(f0, hf, hcur),
            crop(screen0, hf, hcur),
            crop(diag0, hf, hcur),
            crop(m0, hf, hcur),
            1.0,
        )
        hcur -= 1
    indicator = crop(u, hcur, 0)
    return (indicator, density_field)


def solution(mesh):
    placed = (
        P("space", "sub", None, None, None, None, None),
        P("space", "sub", None, None, None, None, None),
        P("space", "sub", None, None, None, None),
        P("space", "sub", None, None, None),
        P("space", "sub", None, None, None),
    )
    return jax.shard_map(
        on_device,
        mesh=mesh,
        in_specs=placed,
        out_specs=(P("space", "sub", None), P("space", "sub", None)),
        check_vma=False,
    )
```

```python
import jax
import jax.numpy as jnp
from jax import lax
from jax.sharding import PartitionSpec as P

BRICK = 8
CX = 16
CY = 16
CZ = 128
LEVELS = 4
SWEEPS = 2
COARSE = 8

screen_weight = 0.05
relax_weight = 0.8

HALO0 = 4
HALO1 = 4


def exchange(x, width, dim_x, dim_y):
    for axis, dim in (("space", dim_x), ("sub", dim_y)):
        devices = lax.axis_size(axis)
        length = x.shape[dim]
        up = [(i, i + 1) for i in range(devices - 1)]
        down = [(j, i) for i, j in up]
        last = lax.slice_in_dim(x, length - width, length, axis=dim)
        first = lax.slice_in_dim(x, 0, width, axis=dim)
        before = lax.ppermute(last, axis, up)
        after = lax.ppermute(first, axis, down)
        x = jnp.concatenate([before, x, after], axis=dim)
    return x


def crop(x, h_from, h_to):
    d = h_from - h_to
    if d == 0:
        return x
    return x[d:-d, d:-d]


def inside_mask(nx, ny, nz, halo):
    dev_x = lax.axis_index("space")
    dev_y = lax.axis_index("sub")
    total_x = lax.axis_size("space") * nx
    total_y = lax.axis_size("sub") * ny
    gx = lax.broadcasted_iota(jnp.int32, (nx + 2 * halo, ny + 2 * halo, nz), 0) + dev_x * nx - halo
    gy = lax.broadcasted_iota(jnp.int32, (nx + 2 * halo, ny + 2 * halo, nz), 1) + dev_y * ny - halo
    ok = (gx >= 0) & (gx < total_x) & (gy >= 0) & (gy < total_y)
    return ok.astype(jnp.float32)


def operate_ext(u, screen_c, scale):
    c = u[1:-1, 1:-1, :]
    zp = jnp.pad(c, ((0, 0), (0, 0), (1, 1)))
    total = u[2:, 1:-1] + u[:-2, 1:-1]
    total = total + u[1:-1, 2:] + u[1:-1, :-2]
    total = total + zp[:, :, 2:] + zp[:, :, :-2]
    return (6.0 * c - total) * scale + screen_c * c


def sweep_ext(u, h, f, screen, diag, mask, scale):
    fc, sc, dc = crop(f, h, h - 1), crop(screen, h, h - 1), crop(diag, h, h - 1)
    new = crop(u, h, h - 1) + relax_weight * (fc - operate_ext(u, sc, scale)) / dc
    return new * crop(mask, h, h - 1)


def pair_matrix(n):
    rows = lax.broadcasted_iota(jnp.int32, (n, n // 2), 0) // 2
    cols = lax.broadcasted_iota(jnp.int32, (n, n // 2), 1)
    return (rows == cols).astype(jnp.float32)


def restrict(field):
    sx, sy, sz = field.shape
    zs = jnp.dot(
        field.reshape(sx * sy, sz), pair_matrix(sz), precision=lax.Precision.HIGHEST
    ).reshape(sx, sy, sz // 2)
    xs = zs.reshape(sx // 2, 2, sy, sz // 2).sum(axis=1)
    ys = xs.reshape(sx // 2, sy // 2, 2, sz // 2).sum(axis=2)
    return ys * 0.125


def prolong(field):
    sx, sy, sz = field.shape
    zs = jnp.dot(
        field.reshape(sx * sy, sz), pair_matrix(2 * sz).T, precision=lax.Precision.HIGHEST
    ).reshape(sx, sy, 2 * sz)
    return jnp.repeat(jnp.repeat(zs, 2, axis=0), 2, axis=1)


def neighbours(padded):
    total = padded[2:, 1:-1, 1:-1] + padded[:-2, 1:-1, 1:-1]
    total = total + padded[1:-1, 2:, 1:-1] + padded[1:-1, :-2, 1:-1]
    return total + padded[1:-1, 1:-1, 2:] + padded[1:-1, 1:-1, :-2]


def operate(field, screen, level_index):
    return (6.0 * field - neighbours(jnp.pad(field, 1))) * (0.25**level_index) + screen * field


def sweep(field, forcing, screen, diagonal, level_index):
    return field + relax_weight * (forcing - operate(field, screen, level_index)) / diagonal


def vcycle_global(forcing, level_index, screens):
    screen = screens[level_index]
    diagonal = 6.0 * (0.25**level_index) + screen
    field = relax_weight * forcing / diagonal
    if level_index == LEVELS - 1:
        for _ in range(COARSE - 1):
            field = sweep(field, forcing, screen, diagonal, level_index)
        return field
    for _ in range(SWEEPS - 1):
        field = sweep(field, forcing, screen, diagonal, level_index)
    residual = forcing - operate(field, screen, level_index)
    correction = vcycle_global(restrict(residual), level_index + 1, screens)
    field = field + prolong(correction)
    for _ in range(SWEEPS):
        field = sweep(field, forcing, screen, diagonal, level_index)
    return field


def splat(packed):
    tiles, _, slots = packed.shape
    centers = jnp.arange(BRICK, dtype=jnp.float32) + 0.5
    wx, wy, wz = [
        jnp.maximum(0.0, 1.0 - jnp.abs(packed[:, row, None, :] - centers[None, :, None]))
        for row in range(3)
    ]
    planar = (wx[:, :, None, :] * wy[:, None, :, :]).reshape(tiles, BRICK * BRICK, slots)
    loaded = (packed[:, 3:7, None, :] * wz[:, None, :, :]).reshape(tiles, 4 * BRICK, slots)
    partials = jnp.einsum("tbs,tas->tba", loaded, planar, precision=lax.Precision.HIGH)
    brick_total = CX // BRICK * (CY // BRICK) * (CZ // BRICK)
    brick_row = packed[:, 7, :brick_total]
    numbers = lax.broadcasted_iota(jnp.float32, (tiles, brick_total), 1)
    onehot = (brick_row == numbers).astype(jnp.float32)
    sums = jnp.einsum("tk,tba->kba", onehot, partials, precision=lax.Precision.HIGH)
    return sums


def gather_all(block, space_count, sub_count):
    channels, nx, ny, nz = block.shape
    devices = space_count * sub_count
    flat = block.reshape(1, -1, 128)
    sent = jnp.broadcast_to(flat, (devices,) + flat.shape[1:])
    every = lax.all_to_all(sent, ("space", "sub"), 0, 0, tiled=True)
    every = every.reshape(space_count, sub_count, channels, nx, ny, nz)
    every = every.transpose(2, 0, 3, 1, 4, 5)
    return every.reshape(channels, space_count * nx, sub_count * ny, nz)


def to_grid(sums):
    shaped = sums.reshape(CX // BRICK, CY // BRICK, CZ // BRICK, 4, BRICK, BRICK, BRICK)
    return shaped.transpose(3, 0, 5, 1, 6, 2, 4).reshape(4, CX, CY, CZ)


def on_device(offsets, normals, density, tile_brick, tile_count):
    space_count = lax.axis_size("space")
    sub_count = lax.axis_size("sub")
    devices = space_count * sub_count
    tiles_each = offsets.shape[4]
    slot_total = offsets.shape[6]

    slot_numbers = lax.broadcasted_iota(jnp.int32, (devices, tiles_each, 1, slot_total), 3)
    live = (slot_numbers < tile_count.reshape(devices, tiles_each, 1, 1)).astype(jnp.float32)
    samples = jnp.concatenate(
        [
            normals.reshape(devices, tiles_each, 3, slot_total),
            density.reshape(devices, tiles_each, 1, slot_total),
        ],
        axis=2,
    ) * live
    brick_row = jnp.broadcast_to(
        tile_brick.reshape(devices, tiles_each, 1, 1).astype(jnp.float32),
        (devices, tiles_each, 1, slot_total),
    )
    packed = jnp.concatenate(
        [offsets.reshape(devices, tiles_each, 3, slot_total), samples, brick_row], axis=2
    )
    received = lax.all_to_all(packed, ("space", "sub"), 0, 0, tiled=True)
    sums = splat(received.reshape(devices * tiles_each, 8, slot_total))
    grid = to_grid(sums)
    density_field = grid[3]

    h0 = HALO0
    g = exchange(grid, h0, 1, 2)
    vx, vy, vz, rho0 = g[0], g[1], g[2], g[3]
    mask0 = inside_mask(CX, CY, CZ, h0)
    hf = h0 - 1
    vzc = jnp.pad(crop(vz, h0, hf), ((0, 0), (0, 0), (1, 1)))
    change = vx[2:, 1:-1] - vx[:-2, 1:-1] + (vy[1:-1, 2:] - vy[1:-1, :-2])
    change = change + (vzc[:, :, 2:] - vzc[:, :, :-2])
    m0 = crop(mask0, h0, hf)
    f0 = -0.5 * change * m0
    screen0 = screen_weight * crop(rho0, h0, hf)
    diag0 = 6.0 + screen0
    u = relax_weight * f0 / diag0 * m0
    u = sweep_ext(u, hf, f0, screen0, diag0, m0, 1.0)
    hu0 = hf - 1
    residual0 = crop(f0, hf, 0) - operate_ext(
        crop(u, hu0, 1), crop(screen0, hf, 0), 1.0
    )

    h1 = HALO1
    f1 = restrict(residual0)
    rho1 = restrict(density_field)
    nx1, ny1, nz1 = f1.shape
    both = exchange(jnp.stack([f1, rho1]), h1, 1, 2)
    f1e, rho1e = both[0], both[1]
    mask1 = inside_mask(nx1, ny1, nz1, h1)
    scale1 = 0.25
    screen1 = screen_weight * rho1e
    diag1 = 6.0 * scale1 + screen1
    u1 = relax_weight * f1e / diag1 * mask1
    u1 = sweep_ext(u1, h1, f1e, screen1, diag1, mask1, scale1)
    hu1 = h1 - 1
    residual1 = crop(f1e, h1, 0) - operate_ext(crop(u1, hu1, 1), crop(screen1, h1, 0), scale1)

    f2 = restrict(residual1)
    nx2, ny2, nz2 = f2.shape

    rho2 = restrict(rho1)
    both2 = gather_all(jnp.stack([f2, rho2]), space_count, sub_count)
    f2g, rho2g = both2[0], both2[1]
    rho3g = restrict(rho2g)
    screens = [None, None, screen_weight * rho2g, screen_weight * rho3g]
    c2g = vcycle_global(f2g, 2, screens)
    hc2 = (hu1 + 1) // 2
    c2p = jnp.pad(c2g, ((hc2, hc2), (hc2, hc2), (0, 0)))
    c2 = lax.dynamic_slice(
        c2p,
        (lax.axis_index("space") * nx2, lax.axis_index("sub") * ny2, 0),
        (nx2 + 2 * hc2, ny2 + 2 * hc2, nz2),
    )

    u1 = u1 + crop(prolong(c2), 2 * hc2, hu1)
    hcur = hu1
    while hcur > 1:
        u1 = sweep_ext(
            u1,
            hcur,
            crop(f1e, h1, hcur),
            crop(screen1, h1, hcur),
            crop(diag1, h1, hcur),
            crop(mask1, h1, hcur),
            scale1,
        )
        hcur -= 1
    c1 = u1

    u = u + crop(prolong(c1), 2, hu0)
    hcur = hu0
    for _ in range(SWEEPS):
        u = sweep_ext(
            u,
            hcur,
            crop(f0, hf, hcur),
            crop(screen0, hf, hcur),
            crop(diag0, hf, hcur),
            crop(m0, hf, hcur),
            1.0,
        )
        hcur -= 1
    indicator = crop(u, hcur, 0)
    return (indicator, density_field)


def solution(mesh):
    placed = (
        P("space", "sub", None, None, None, None, None),
        P("space", "sub", None, None, None, None, None),
        P("space", "sub", None, None, None, None),
        P("space", "sub", None, None, None),
        P("space", "sub", None, None, None),
    )
    return jax.shard_map(
        on_device,
        mesh=mesh,
        in_specs=placed,
        out_specs=(P("space", "sub", None), P("space", "sub", None)),
        check_vma=False,
    )
```

```python
import jax
import jax.numpy as jnp
from jax import lax
from jax.sharding import PartitionSpec as P

BRICK = 8
CX = 16
CY = 16
CZ = 128
LEVELS = 4
SWEEPS = 2
COARSE = 8

screen_weight = 0.05
relax_weight = 0.8

HALO0 = 4
HALO1 = 4


def exchange(x, width, dim_x, dim_y):
    for axis, dim in (("space", dim_x), ("sub", dim_y)):
        devices = lax.axis_size(axis)
        length = x.shape[dim]
        up = [(i, i + 1) for i in range(devices - 1)]
        down = [(j, i) for i, j in up]
        last = lax.slice_in_dim(x, length - width, length, axis=dim)
        first = lax.slice_in_dim(x, 0, width, axis=dim)
        before = lax.ppermute(last, axis, up)
        after = lax.ppermute(first, axis, down)
        x = jnp.concatenate([before, x, after], axis=dim)
    return x


def crop(x, h_from, h_to):
    d = h_from - h_to
    if d == 0:
        return x
    return x[d:-d, d:-d]


def inside_mask(nx, ny, nz, halo):
    dev_x = lax.axis_index("space")
    dev_y = lax.axis_index("sub")
    total_x = lax.axis_size("space") * nx
    total_y = lax.axis_size("sub") * ny
    gx = lax.broadcasted_iota(jnp.int32, (nx + 2 * halo, ny + 2 * halo, nz), 0) + dev_x * nx - halo
    gy = lax.broadcasted_iota(jnp.int32, (nx + 2 * halo, ny + 2 * halo, nz), 1) + dev_y * ny - halo
    ok = (gx >= 0) & (gx < total_x) & (gy >= 0) & (gy < total_y)
    return ok.astype(jnp.float32)


def operate_ext(u, screen_c, scale):
    c = u[1:-1, 1:-1, :]
    zp = jnp.pad(c, ((0, 0), (0, 0), (1, 1)))
    total = u[2:, 1:-1] + u[:-2, 1:-1]
    total = total + u[1:-1, 2:] + u[1:-1, :-2]
    total = total + zp[:, :, 2:] + zp[:, :, :-2]
    return (6.0 * c - total) * scale + screen_c * c


def sweep_ext(u, h, f, screen, diag, mask, scale):
    fc, sc, dc = crop(f, h, h - 1), crop(screen, h, h - 1), crop(diag, h, h - 1)
    new = crop(u, h, h - 1) + relax_weight * (fc - operate_ext(u, sc, scale)) / dc
    return new * crop(mask, h, h - 1)


def pair_matrix(n):
    rows = lax.broadcasted_iota(jnp.int32, (n, n // 2), 0) // 2
    cols = lax.broadcasted_iota(jnp.int32, (n, n // 2), 1)
    return (rows == cols).astype(jnp.float32)


def restrict(field):
    sx, sy, sz = field.shape
    zs = jnp.dot(
        field.reshape(sx * sy, sz), pair_matrix(sz), precision=lax.Precision.HIGHEST
    ).reshape(sx, sy, sz // 2)
    xs = zs.reshape(sx // 2, 2, sy, sz // 2).sum(axis=1)
    ys = xs.reshape(sx // 2, sy // 2, 2, sz // 2).sum(axis=2)
    return ys * 0.125


def prolong(field):
    sx, sy, sz = field.shape
    zs = jnp.dot(
        field.reshape(sx * sy, sz), pair_matrix(2 * sz).T, precision=lax.Precision.HIGHEST
    ).reshape(sx, sy, 2 * sz)
    return jnp.repeat(jnp.repeat(zs, 2, axis=0), 2, axis=1)


def neighbours(padded):
    total = padded[2:, 1:-1, 1:-1] + padded[:-2, 1:-1, 1:-1]
    total = total + padded[1:-1, 2:, 1:-1] + padded[1:-1, :-2, 1:-1]
    return total + padded[1:-1, 1:-1, 2:] + padded[1:-1, 1:-1, :-2]


def operate(field, screen, level_index):
    return (6.0 * field - neighbours(jnp.pad(field, 1))) * (0.25**level_index) + screen * field


def sweep(field, forcing, screen, diagonal, level_index):
    return field + relax_weight * (forcing - operate(field, screen, level_index)) / diagonal


def vcycle_global(forcing, level_index, screens):
    screen = screens[level_index]
    diagonal = 6.0 * (0.25**level_index) + screen
    field = relax_weight * forcing / diagonal
    if level_index == LEVELS - 1:
        for _ in range(COARSE - 1):
            field = sweep(field, forcing, screen, diagonal, level_index)
        return field
    for _ in range(SWEEPS - 1):
        field = sweep(field, forcing, screen, diagonal, level_index)
    residual = forcing - operate(field, screen, level_index)
    correction = vcycle_global(restrict(residual), level_index + 1, screens)
    field = field + prolong(correction)
    for _ in range(SWEEPS):
        field = sweep(field, forcing, screen, diagonal, level_index)
    return field


def lane_pairs(ny, nz):
    rows = lax.broadcasted_iota(jnp.int32, (ny * nz, ny * nz // 4), 0)
    cols = lax.broadcasted_iota(jnp.int32, (ny * nz, ny * nz // 4), 1)
    coarse = (rows // nz // 2) * (nz // 2) + (rows % nz) // 2
    return (coarse == cols).astype(jnp.float32)


def restrict2d(field, ny, nz):
    sx, lanes = field.shape
    xs = field.reshape(sx // 2, 2, lanes).sum(axis=1)
    ys = jnp.dot(xs, lane_pairs(ny, nz), precision=lax.Precision.HIGHEST)
    return ys * 0.125


def prolong2d(field, ny, nz):
    spread = jnp.dot(field, lane_pairs(ny, nz).T, precision=lax.Precision.HIGHEST)
    return jnp.repeat(spread, 2, axis=0)


def operate2d(u, screen, scale, nz):
    sx, lanes = u.shape
    zi = lax.broadcasted_iota(jnp.int32, (sx, lanes), 1) % nz
    xp = jnp.pad(u, ((0, 1), (0, 0)))[1:]
    xm = jnp.pad(u, ((1, 0), (0, 0)))[:-1]
    yp = jnp.pad(u, ((0, 0), (0, nz)))[:, nz:]
    ym = jnp.pad(u, ((0, 0), (nz, 0)))[:, :-nz]
    zp = jnp.where(zi < nz - 1, jnp.pad(u, ((0, 0), (0, 1)))[:, 1:], 0.0)
    zm = jnp.where(zi > 0, jnp.pad(u, ((0, 0), (1, 0)))[:, :-1], 0.0)
    total = xp + xm
    total = total + yp + ym
    total = total + zp + zm
    return (6.0 * u - total) * scale + screen * u


def vcycle2d(forcing, level_index, screens, shapes):
    ny, nz = shapes[level_index]
    screen = screens[level_index]
    scale = 0.25**level_index
    diagonal = 6.0 * scale + screen
    field = relax_weight * forcing / diagonal

    def sweep2d(u):
        return u + relax_weight * (forcing - operate2d(u, screen, scale, nz)) / diagonal

    if level_index == LEVELS - 1:
        for _ in range(COARSE - 1):
            field = sweep2d(field)
        return field
    for _ in range(SWEEPS - 1):
        field = sweep2d(field)
    residual = forcing - operate2d(field, screen, scale, nz)
    correction = vcycle2d(restrict2d(residual, ny, nz), level_index + 1, screens, shapes)
    field = field + prolong2d(correction, ny, nz)
    for _ in range(SWEEPS):
        field = sweep2d(field)
    return field


def coarse_solve(f2g, rho2g):
    sx, ny, nz = f2g.shape
    f = f2g.reshape(sx, ny * nz)
    rho2 = rho2g.reshape(sx, ny * nz)
    rho3 = restrict2d(rho2, ny, nz)
    screens = [None, None, screen_weight * rho2, screen_weight * rho3]
    shapes = [None, None, (ny, nz), (ny // 2, nz // 2)]
    return vcycle2d(f, 2, screens, shapes).reshape(sx, ny, nz)


def splat(packed):
    tiles, _, slots = packed.shape
    centers = jnp.arange(BRICK, dtype=jnp.float32) + 0.5
    wx, wy, wz = [
        jnp.maximum(0.0, 1.0 - jnp.abs(packed[:, row, None, :] - centers[None, :, None]))
        for row in range(3)
    ]
    planar = (wx[:, :, None, :] * wy[:, None, :, :]).reshape(tiles, BRICK * BRICK, slots)
    loaded = (packed[:, 3:7, None, :] * wz[:, None, :, :]).reshape(tiles, 4 * BRICK, slots)
    partials = jnp.einsum("tbs,tas->tba", loaded, planar, precision=lax.Precision.HIGH)
    brick_total = CX // BRICK * (CY // BRICK) * (CZ // BRICK)
    brick_row = packed[:, 7, :brick_total]
    numbers = lax.broadcasted_iota(jnp.float32, (tiles, brick_total), 1)
    onehot = (brick_row == numbers).astype(jnp.float32)
    sums = jnp.einsum("tk,tba->kba", onehot, partials, precision=lax.Precision.HIGH)
    return sums


def gather_all(block, space_count, sub_count):
    channels, nx, ny, nz = block.shape
    devices = space_count * sub_count
    flat = block.reshape(1, -1, 128)
    sent = jnp.broadcast_to(flat, (devices,) + flat.shape[1:])
    every = lax.all_to_all(sent, ("space", "sub"), 0, 0, tiled=True)
    every = every.reshape(space_count, sub_count, channels, nx, ny, nz)
    every = every.transpose(2, 0, 3, 1, 4, 5)
    return every.reshape(channels, space_count * nx, sub_count * ny, nz)


def to_grid(sums):
    shaped = sums.reshape(CX // BRICK, CY // BRICK, CZ // BRICK, 4, BRICK, BRICK, BRICK)
    return shaped.transpose(3, 0, 5, 1, 6, 2, 4).reshape(4, CX, CY, CZ)


def on_device(offsets, normals, density, tile_brick, tile_count):
    space_count = lax.axis_size("space")
    sub_count = lax.axis_size("sub")
    devices = space_count * sub_count
    tiles_each = offsets.shape[4]
    slot_total = offsets.shape[6]

    slot_numbers = lax.broadcasted_iota(jnp.int32, (devices, tiles_each, 1, slot_total), 3)
    live = (slot_numbers < tile_count.reshape(devices, tiles_each, 1, 1)).astype(jnp.float32)
    samples = jnp.concatenate(
        [
            normals.reshape(devices, tiles_each, 3, slot_total),
            density.reshape(devices, tiles_each, 1, slot_total),
        ],
        axis=2,
    ) * live
    brick_row = jnp.broadcast_to(
        tile_brick.reshape(devices, tiles_each, 1, 1).astype(jnp.float32),
        (devices, tiles_each, 1, slot_total),
    )
    packed = jnp.concatenate(
        [offsets.reshape(devices, tiles_each, 3, slot_total), samples, brick_row], axis=2
    )
    received = lax.all_to_all(packed, ("space", "sub"), 0, 0, tiled=True)
    sums = splat(received.reshape(devices * tiles_each, 8, slot_total))
    grid = to_grid(sums)
    density_field = grid[3]

    h0 = HALO0
    g = exchange(grid, h0, 1, 2)
    vx, vy, vz, rho0 = g[0], g[1], g[2], g[3]
    mask0 = inside_mask(CX, CY, CZ, h0)
    hf = h0 - 1
    vzc = jnp.pad(crop(vz, h0, hf), ((0, 0), (0, 0), (1, 1)))
    change = vx[2:, 1:-1] - vx[:-2, 1:-1] + (vy[1:-1, 2:] - vy[1:-1, :-2])
    change = change + (vzc[:, :, 2:] - vzc[:, :, :-2])
    m0 = crop(mask0, h0, hf)
    f0 = -0.5 * change * m0
    screen0 = screen_weight * crop(rho0, h0, hf)
    diag0 = 6.0 + screen0
    u = relax_weight * f0 / diag0 * m0
    u = sweep_ext(u, hf, f0, screen0, diag0, m0, 1.0)
    hu0 = hf - 1
    residual0 = crop(f0, hf, 0) - operate_ext(
        crop(u, hu0, 1), crop(screen0, hf, 0), 1.0
    )

    h1 = HALO1
    f1 = restrict(residual0)
    rho1 = restrict(density_field)
    nx1, ny1, nz1 = f1.shape
    both = exchange(jnp.stack([f1, rho1]), h1, 1, 2)
    f1e, rho1e = both[0], both[1]
    mask1 = inside_mask(nx1, ny1, nz1, h1)
    scale1 = 0.25
    screen1 = screen_weight * rho1e
    diag1 = 6.0 * scale1 + screen1
    u1 = relax_weight * f1e / diag1 * mask1
    u1 = sweep_ext(u1, h1, f1e, screen1, diag1, mask1, scale1)
    hu1 = h1 - 1
    residual1 = crop(f1e, h1, 0) - operate_ext(crop(u1, hu1, 1), crop(screen1, h1, 0), scale1)

    f2 = restrict(residual1)
    nx2, ny2, nz2 = f2.shape

    rho2 = restrict(rho1)
    both2 = gather_all(jnp.stack([f2, rho2]), space_count, sub_count)
    f2g, rho2g = both2[0], both2[1]
    c2g = coarse_solve(f2g, rho2g)
    hc2 = (hu1 + 1) // 2
    c2p = jnp.pad(c2g, ((hc2, hc2), (hc2, hc2), (0, 0)))
    c2 = lax.dynamic_slice(
        c2p,
        (lax.axis_index("space") * nx2, lax.axis_index("sub") * ny2, 0),
        (nx2 + 2 * hc2, ny2 + 2 * hc2, nz2),
    )

    u1 = u1 + crop(prolong(c2), 2 * hc2, hu1)
    hcur = hu1
    while hcur > 1:
        u1 = sweep_ext(
            u1,
            hcur,
            crop(f1e, h1, hcur),
            crop(screen1, h1, hcur),
            crop(diag1, h1, hcur),
            crop(mask1, h1, hcur),
            scale1,
        )
        hcur -= 1
    c1 = u1

    u = u + crop(prolong(c1), 2, hu0)
    hcur = hu0
    for _ in range(SWEEPS):
        u = sweep_ext(
            u,
            hcur,
            crop(f0, hf, hcur),
            crop(screen0, hf, hcur),
            crop(diag0, hf, hcur),
            crop(m0, hf, hcur),
            1.0,
        )
        hcur -= 1
    indicator = crop(u, hcur, 0)
    return (indicator, density_field)


def solution(mesh):
    placed = (
        P("space", "sub", None, None, None, None, None),
        P("space", "sub", None, None, None, None, None),
        P("space", "sub", None, None, None, None),
        P("space", "sub", None, None, None),
        P("space", "sub", None, None, None),
    )
    return jax.shard_map(
        on_device,
        mesh=mesh,
        in_specs=placed,
        out_specs=(P("space", "sub", None), P("space", "sub", None)),
        check_vma=False,
    )
```

```python
import jax
import jax.numpy as jnp
from jax import lax
from jax.sharding import PartitionSpec as P

BRICK = 8
CX = 16
CY = 16
CZ = 128
LEVELS = 4
SWEEPS = 2
COARSE = 8

screen_weight = 0.05
relax_weight = 0.8

HALO0 = 4
HALO1 = 4


def exchange(x, width, dim_x, dim_y):
    for axis, dim in (("space", dim_x), ("sub", dim_y)):
        devices = lax.axis_size(axis)
        length = x.shape[dim]
        up = [(i, i + 1) for i in range(devices - 1)]
        down = [(j, i) for i, j in up]
        last = lax.slice_in_dim(x, length - width, length, axis=dim)
        first = lax.slice_in_dim(x, 0, width, axis=dim)
        before = lax.ppermute(last, axis, up)
        after = lax.ppermute(first, axis, down)
        x = jnp.concatenate([before, x, after], axis=dim)
    return x


def crop(x, h_from, h_to):
    d = h_from - h_to
    if d == 0:
        return x
    return x[d:-d, d:-d]


def inside_mask(nx, ny, nz, halo):
    dev_x = lax.axis_index("space")
    dev_y = lax.axis_index("sub")
    total_x = lax.axis_size("space") * nx
    total_y = lax.axis_size("sub") * ny
    gx = lax.broadcasted_iota(jnp.int32, (nx + 2 * halo, ny + 2 * halo, nz), 0) + dev_x * nx - halo
    gy = lax.broadcasted_iota(jnp.int32, (nx + 2 * halo, ny + 2 * halo, nz), 1) + dev_y * ny - halo
    ok = (gx >= 0) & (gx < total_x) & (gy >= 0) & (gy < total_y)
    return ok.astype(jnp.float32)


def operate_ext(u, screen_c, scale):
    c = u[1:-1, 1:-1, :]
    zp = jnp.pad(c, ((0, 0), (0, 0), (1, 1)))
    total = u[2:, 1:-1] + u[:-2, 1:-1]
    total = total + u[1:-1, 2:] + u[1:-1, :-2]
    total = total + zp[:, :, 2:] + zp[:, :, :-2]
    return (6.0 * c - total) * scale + screen_c * c


def sweep_ext(u, h, f, screen, diag, mask, scale):
    fc, sc, dc = crop(f, h, h - 1), crop(screen, h, h - 1), crop(diag, h, h - 1)
    new = crop(u, h, h - 1) + relax_weight * (fc - operate_ext(u, sc, scale)) / dc
    return new * crop(mask, h, h - 1)


def pair_matrix(n):
    rows = lax.broadcasted_iota(jnp.int32, (n, n // 2), 0) // 2
    cols = lax.broadcasted_iota(jnp.int32, (n, n // 2), 1)
    return (rows == cols).astype(jnp.float32)


def restrict(field):
    sx, sy, sz = field.shape
    zs = jnp.dot(
        field.reshape(sx * sy, sz), pair_matrix(sz), precision=lax.Precision.HIGHEST
    ).reshape(sx, sy, sz // 2)
    xs = zs.reshape(sx // 2, 2, sy, sz // 2).sum(axis=1)
    ys = xs.reshape(sx // 2, sy // 2, 2, sz // 2).sum(axis=2)
    return ys * 0.125


def prolong(field):
    sx, sy, sz = field.shape
    zs = jnp.dot(
        field.reshape(sx * sy, sz), pair_matrix(2 * sz).T, precision=lax.Precision.HIGHEST
    ).reshape(sx, sy, 2 * sz)
    return jnp.repeat(jnp.repeat(zs, 2, axis=0), 2, axis=1)


def neighbours(padded):
    total = padded[2:, 1:-1, 1:-1] + padded[:-2, 1:-1, 1:-1]
    total = total + padded[1:-1, 2:, 1:-1] + padded[1:-1, :-2, 1:-1]
    return total + padded[1:-1, 1:-1, 2:] + padded[1:-1, 1:-1, :-2]


def operate(field, screen, level_index):
    return (6.0 * field - neighbours(jnp.pad(field, 1))) * (0.25**level_index) + screen * field


def sweep(field, forcing, screen, diagonal, level_index):
    return field + relax_weight * (forcing - operate(field, screen, level_index)) / diagonal


def vcycle_global(forcing, level_index, screens):
    screen = screens[level_index]
    diagonal = 6.0 * (0.25**level_index) + screen
    field = relax_weight * forcing / diagonal
    if level_index == LEVELS - 1:
        for _ in range(COARSE - 1):
            field = sweep(field, forcing, screen, diagonal, level_index)
        return field
    for _ in range(SWEEPS - 1):
        field = sweep(field, forcing, screen, diagonal, level_index)
    residual = forcing - operate(field, screen, level_index)
    correction = vcycle_global(restrict(residual), level_index + 1, screens)
    field = field + prolong(correction)
    for _ in range(SWEEPS):
        field = sweep(field, forcing, screen, diagonal, level_index)
    return field


def lane_pairs(ny, nz):
    rows = lax.broadcasted_iota(jnp.int32, (ny * nz, ny * nz // 4), 0)
    cols = lax.broadcasted_iota(jnp.int32, (ny * nz, ny * nz // 4), 1)
    coarse = (rows // nz // 2) * (nz // 2) + (rows % nz) // 2
    return (coarse == cols).astype(jnp.float32)


def restrict2d(field, ny, nz):
    sx, lanes = field.shape
    xs = field.reshape(sx // 2, 2, lanes).sum(axis=1)
    ys = jnp.dot(xs, lane_pairs(ny, nz), precision=lax.Precision.HIGHEST)
    return ys * 0.125


def prolong2d(field, ny, nz):
    spread = jnp.dot(field, lane_pairs(ny, nz).T, precision=lax.Precision.HIGHEST)
    return jnp.repeat(spread, 2, axis=0)


def operate2d(u, screen, scale, nz):
    sx, lanes = u.shape
    zi = lax.broadcasted_iota(jnp.int32, (sx, lanes), 1) % nz
    xp = jnp.pad(u, ((0, 1), (0, 0)))[1:]
    xm = jnp.pad(u, ((1, 0), (0, 0)))[:-1]
    yp = jnp.pad(u, ((0, 0), (0, nz)))[:, nz:]
    ym = jnp.pad(u, ((0, 0), (nz, 0)))[:, :-nz]
    zp = jnp.where(zi < nz - 1, jnp.pad(u, ((0, 0), (0, 1)))[:, 1:], 0.0)
    zm = jnp.where(zi > 0, jnp.pad(u, ((0, 0), (1, 0)))[:, :-1], 0.0)
    total = xp + xm
    total = total + yp + ym
    total = total + zp + zm
    return (6.0 * u - total) * scale + screen * u


def vcycle2d(forcing, level_index, screens, shapes):
    ny, nz = shapes[level_index]
    screen = screens[level_index]
    scale = 0.25**level_index
    diagonal = 6.0 * scale + screen
    field = relax_weight * forcing / diagonal

    def sweep2d(u):
        return u + relax_weight * (forcing - operate2d(u, screen, scale, nz)) / diagonal

    if level_index == LEVELS - 1:
        for _ in range(COARSE - 1):
            field = sweep2d(field)
        return field
    for _ in range(SWEEPS - 1):
        field = sweep2d(field)
    residual = forcing - operate2d(field, screen, scale, nz)
    correction = vcycle2d(restrict2d(residual, ny, nz), level_index + 1, screens, shapes)
    field = field + prolong2d(correction, ny, nz)
    for _ in range(SWEEPS):
        field = sweep2d(field)
    return field


def coarse_solve(f, rho2, ny, nz):
    rho3 = restrict2d(rho2, ny, nz)
    screens = [None, None, screen_weight * rho2, screen_weight * rho3]
    shapes = [None, None, (ny, nz), (ny // 2, nz // 2)]
    return vcycle2d(f, 2, screens, shapes)


def splat(packed):
    tiles, _, slots = packed.shape
    centers = jnp.arange(BRICK, dtype=jnp.float32) + 0.5
    wx, wy, wz = [
        jnp.maximum(0.0, 1.0 - jnp.abs(packed[:, row, None, :] - centers[None, :, None]))
        for row in range(3)
    ]
    planar = (wx[:, :, None, :] * wy[:, None, :, :]).reshape(tiles, BRICK * BRICK, slots)
    loaded = (packed[:, 3:7, None, :] * wz[:, None, :, :]).reshape(tiles, 4 * BRICK, slots)
    partials = jnp.einsum("tbs,tas->tba", loaded, planar, precision=lax.Precision.HIGH)
    brick_total = CX // BRICK * (CY // BRICK) * (CZ // BRICK)
    brick_row = packed[:, 7, :brick_total]
    numbers = lax.broadcasted_iota(jnp.float32, (tiles, brick_total), 1)
    onehot = (brick_row == numbers).astype(jnp.float32)
    sums = jnp.einsum("tk,tba->kba", onehot, partials, precision=lax.Precision.HIGH)
    return sums


def gather_all(block, space_count, sub_count):
    channels, nx, ny, nz = block.shape
    devices = space_count * sub_count
    flat = block.reshape(1, channels * nx, ny * nz)
    sent = jnp.broadcast_to(flat, (devices,) + flat.shape[1:])
    every = lax.all_to_all(sent, ("space", "sub"), 0, 0, tiled=True)
    every = every.reshape(space_count, sub_count, channels, nx, ny * nz)
    every = every.transpose(2, 0, 3, 1, 4)
    return every.reshape(channels, space_count * nx, sub_count * ny * nz)


def to_grid(sums):
    shaped = sums.reshape(CX // BRICK, CY // BRICK, CZ // BRICK, 4, BRICK, BRICK, BRICK)
    return shaped.transpose(3, 0, 5, 1, 6, 2, 4).reshape(4, CX, CY, CZ)


def on_device(offsets, normals, density, tile_brick, tile_count):
    space_count = lax.axis_size("space")
    sub_count = lax.axis_size("sub")
    devices = space_count * sub_count
    tiles_each = offsets.shape[4]
    slot_total = offsets.shape[6]

    slot_numbers = lax.broadcasted_iota(jnp.int32, (devices, tiles_each, 1, slot_total), 3)
    live = (slot_numbers < tile_count.reshape(devices, tiles_each, 1, 1)).astype(jnp.float32)
    samples = jnp.concatenate(
        [
            normals.reshape(devices, tiles_each, 3, slot_total),
            density.reshape(devices, tiles_each, 1, slot_total),
        ],
        axis=2,
    ) * live
    brick_row = jnp.broadcast_to(
        tile_brick.reshape(devices, tiles_each, 1, 1).astype(jnp.float32),
        (devices, tiles_each, 1, slot_total),
    )
    packed = jnp.concatenate(
        [offsets.reshape(devices, tiles_each, 3, slot_total), samples, brick_row], axis=2
    )
    received = lax.all_to_all(packed, ("space", "sub"), 0, 0, tiled=True)
    sums = splat(received.reshape(devices * tiles_each, 8, slot_total))
    grid = to_grid(sums)
    density_field = grid[3]

    h0 = HALO0
    g = exchange(grid, h0, 1, 2)
    vx, vy, vz, rho0 = g[0], g[1], g[2], g[3]
    mask0 = inside_mask(CX, CY, CZ, h0)
    hf = h0 - 1
    vzc = jnp.pad(crop(vz, h0, hf), ((0, 0), (0, 0), (1, 1)))
    change = vx[2:, 1:-1] - vx[:-2, 1:-1] + (vy[1:-1, 2:] - vy[1:-1, :-2])
    change = change + (vzc[:, :, 2:] - vzc[:, :, :-2])
    m0 = crop(mask0, h0, hf)
    f0 = -0.5 * change * m0
    screen0 = screen_weight * crop(rho0, h0, hf)
    diag0 = 6.0 + screen0
    u = relax_weight * f0 / diag0 * m0
    u = sweep_ext(u, hf, f0, screen0, diag0, m0, 1.0)
    hu0 = hf - 1
    residual0 = crop(f0, hf, 0) - operate_ext(
        crop(u, hu0, 1), crop(screen0, hf, 0), 1.0
    )

    h1 = HALO1
    f1 = restrict(residual0)
    rho1 = restrict(density_field)
    nx1, ny1, nz1 = f1.shape
    both = exchange(jnp.stack([f1, rho1]), h1, 1, 2)
    f1e, rho1e = both[0], both[1]
    mask1 = inside_mask(nx1, ny1, nz1, h1)
    scale1 = 0.25
    screen1 = screen_weight * rho1e
    diag1 = 6.0 * scale1 + screen1
    u1 = relax_weight * f1e / diag1 * mask1
    u1 = sweep_ext(u1, h1, f1e, screen1, diag1, mask1, scale1)
    hu1 = h1 - 1
    residual1 = crop(f1e, h1, 0) - operate_ext(crop(u1, hu1, 1), crop(screen1, h1, 0), scale1)

    f2 = restrict(residual1)
    nx2, ny2, nz2 = f2.shape

    rho2 = restrict(rho1)
    both2 = gather_all(jnp.stack([f2, rho2]), space_count, sub_count)
    c2g = coarse_solve(both2[0], both2[1], sub_count * ny2, nz2)
    hc2 = (hu1 + 1) // 2
    c2p = jnp.pad(c2g, ((hc2, hc2), (hc2 * nz2, hc2 * nz2)))
    c2 = lax.dynamic_slice(
        c2p,
        (lax.axis_index("space") * nx2, lax.axis_index("sub") * ny2 * nz2),
        (nx2 + 2 * hc2, (ny2 + 2 * hc2) * nz2),
    ).reshape(nx2 + 2 * hc2, ny2 + 2 * hc2, nz2)

    u1 = u1 + crop(prolong(c2), 2 * hc2, hu1)
    hcur = hu1
    while hcur > 1:
        u1 = sweep_ext(
            u1,
            hcur,
            crop(f1e, h1, hcur),
            crop(screen1, h1, hcur),
            crop(diag1, h1, hcur),
            crop(mask1, h1, hcur),
            scale1,
        )
        hcur -= 1
    c1 = u1

    u = u + crop(prolong(c1), 2, hu0)
    hcur = hu0
    for _ in range(SWEEPS):
        u = sweep_ext(
            u,
            hcur,
            crop(f0, hf, hcur),
            crop(screen0, hf, hcur),
            crop(diag0, hf, hcur),
            crop(m0, hf, hcur),
            1.0,
        )
        hcur -= 1
    indicator = crop(u, hcur, 0)
    return (indicator, density_field)


def solution(mesh):
    placed = (
        P("space", "sub", None, None, None, None, None),
        P("space", "sub", None, None, None, None, None),
        P("space", "sub", None, None, None, None),
        P("space", "sub", None, None, None),
        P("space", "sub", None, None, None),
    )
    return jax.shard_map(
        on_device,
        mesh=mesh,
        in_specs=placed,
        out_specs=(P("space", "sub", None), P("space", "sub", None)),
        check_vma=False,
    )
```

```python
import jax
import jax.numpy as jnp
from jax import lax
from jax.sharding import PartitionSpec as P

BRICK = 8
CX = 16
CY = 16
CZ = 128
LEVELS = 4
SWEEPS = 2
COARSE = 8

screen_weight = 0.05
relax_weight = 0.8

HALO0 = 4
HALO1 = 4


def exchange(x, width, dim_x, dim_y):
    spaces = lax.axis_size("space")
    subs = lax.axis_size("sub")

    def part(piece, side, dim):
        length = piece.shape[dim]
        if side < 0:
            return lax.slice_in_dim(piece, length - width, length, axis=dim)
        if side > 0:
            return lax.slice_in_dim(piece, 0, width, axis=dim)
        return piece

    rows = []
    for rx in (-1, 0, 1):
        columns = []
        for ry in (-1, 0, 1):
            piece = part(part(x, rx, dim_x), ry, dim_y)
            if rx or ry:
                perm = [
                    (s * subs + b, (s - rx) * subs + (b - ry))
                    for s in range(spaces)
                    for b in range(subs)
                    if 0 <= s - rx < spaces and 0 <= b - ry < subs
                ]
                piece = lax.ppermute(piece, ("space", "sub"), perm)
            columns.append(piece)
        rows.append(jnp.concatenate(columns, axis=dim_y))
    return jnp.concatenate(rows, axis=dim_x)


def crop(x, h_from, h_to):
    d = h_from - h_to
    if d == 0:
        return x
    return x[d:-d, d:-d]


def inside_mask(nx, ny, nz, halo):
    dev_x = lax.axis_index("space")
    dev_y = lax.axis_index("sub")
    total_x = lax.axis_size("space") * nx
    total_y = lax.axis_size("sub") * ny
    gx = lax.broadcasted_iota(jnp.int32, (nx + 2 * halo, ny + 2 * halo, nz), 0) + dev_x * nx - halo
    gy = lax.broadcasted_iota(jnp.int32, (nx + 2 * halo, ny + 2 * halo, nz), 1) + dev_y * ny - halo
    ok = (gx >= 0) & (gx < total_x) & (gy >= 0) & (gy < total_y)
    return ok.astype(jnp.float32)


def operate_ext(u, screen_c, scale):
    c = u[1:-1, 1:-1, :]
    zp = jnp.pad(c, ((0, 0), (0, 0), (1, 1)))
    total = u[2:, 1:-1] + u[:-2, 1:-1]
    total = total + u[1:-1, 2:] + u[1:-1, :-2]
    total = total + zp[:, :, 2:] + zp[:, :, :-2]
    return (6.0 * c - total) * scale + screen_c * c


def sweep_ext(u, h, f, screen, diag, mask, scale):
    fc, sc, dc = crop(f, h, h - 1), crop(screen, h, h - 1), crop(diag, h, h - 1)
    new = crop(u, h, h - 1) + relax_weight * (fc - operate_ext(u, sc, scale)) / dc
    return new * crop(mask, h, h - 1)


def pair_matrix(n):
    rows = lax.broadcasted_iota(jnp.int32, (n, n // 2), 0) // 2
    cols = lax.broadcasted_iota(jnp.int32, (n, n // 2), 1)
    return (rows == cols).astype(jnp.float32)


def restrict(field):
    sx, sy, sz = field.shape
    zs = jnp.dot(
        field.reshape(sx * sy, sz), pair_matrix(sz), precision=lax.Precision.HIGHEST
    ).reshape(sx, sy, sz // 2)
    xs = zs.reshape(sx // 2, 2, sy, sz // 2).sum(axis=1)
    ys = xs.reshape(sx // 2, sy // 2, 2, sz // 2).sum(axis=2)
    return ys * 0.125


def prolong(field):
    sx, sy, sz = field.shape
    zs = jnp.dot(
        field.reshape(sx * sy, sz), pair_matrix(2 * sz).T, precision=lax.Precision.HIGHEST
    ).reshape(sx, sy, 2 * sz)
    return jnp.repeat(jnp.repeat(zs, 2, axis=0), 2, axis=1)


def neighbours(padded):
    total = padded[2:, 1:-1, 1:-1] + padded[:-2, 1:-1, 1:-1]
    total = total + padded[1:-1, 2:, 1:-1] + padded[1:-1, :-2, 1:-1]
    return total + padded[1:-1, 1:-1, 2:] + padded[1:-1, 1:-1, :-2]


def operate(field, screen, level_index):
    return (6.0 * field - neighbours(jnp.pad(field, 1))) * (0.25**level_index) + screen * field


def sweep(field, forcing, screen, diagonal, level_index):
    return field + relax_weight * (forcing - operate(field, screen, level_index)) / diagonal


def vcycle_global(forcing, level_index, screens):
    screen = screens[level_index]
    diagonal = 6.0 * (0.25**level_index) + screen
    field = relax_weight * forcing / diagonal
    if level_index == LEVELS - 1:
        for _ in range(COARSE - 1):
            field = sweep(field, forcing, screen, diagonal, level_index)
        return field
    for _ in range(SWEEPS - 1):
        field = sweep(field, forcing, screen, diagonal, level_index)
    residual = forcing - operate(field, screen, level_index)
    correction = vcycle_global(restrict(residual), level_index + 1, screens)
    field = field + prolong(correction)
    for _ in range(SWEEPS):
        field = sweep(field, forcing, screen, diagonal, level_index)
    return field


def lane_pairs(ny, nz):
    rows = lax.broadcasted_iota(jnp.int32, (ny * nz, ny * nz // 4), 0)
    cols = lax.broadcasted_iota(jnp.int32, (ny * nz, ny * nz // 4), 1)
    coarse = (rows // nz // 2) * (nz // 2) + (rows % nz) // 2
    return (coarse == cols).astype(jnp.float32)


def restrict2d(field, ny, nz):
    sx, lanes = field.shape
    xs = field.reshape(sx // 2, 2, lanes).sum(axis=1)
    ys = jnp.dot(xs, lane_pairs(ny, nz), precision=lax.Precision.HIGHEST)
    return ys * 0.125


def prolong2d(field, ny, nz):
    spread = jnp.dot(field, lane_pairs(ny, nz).T, precision=lax.Precision.HIGHEST)
    return jnp.repeat(spread, 2, axis=0)


def operate2d(u, screen, scale, nz):
    sx, lanes = u.shape
    zi = lax.broadcasted_iota(jnp.int32, (sx, lanes), 1) % nz
    xp = jnp.pad(u, ((0, 1), (0, 0)))[1:]
    xm = jnp.pad(u, ((1, 0), (0, 0)))[:-1]
    yp = jnp.pad(u, ((0, 0), (0, nz)))[:, nz:]
    ym = jnp.pad(u, ((0, 0), (nz, 0)))[:, :-nz]
    zp = jnp.where(zi < nz - 1, jnp.pad(u, ((0, 0), (0, 1)))[:, 1:], 0.0)
    zm = jnp.where(zi > 0, jnp.pad(u, ((0, 0), (1, 0)))[:, :-1], 0.0)
    total = xp + xm
    total = total + yp + ym
    total = total + zp + zm
    return (6.0 * u - total) * scale + screen * u


def vcycle2d(forcing, level_index, screens, shapes):
    ny, nz = shapes[level_index]
    screen = screens[level_index]
    scale = 0.25**level_index
    diagonal = 6.0 * scale + screen
    field = relax_weight * forcing / diagonal

    def sweep2d(u):
        return u + relax_weight * (forcing - operate2d(u, screen, scale, nz)) / diagonal

    if level_index == LEVELS - 1:
        for _ in range(COARSE - 1):
            field = sweep2d(field)
        return field
    for _ in range(SWEEPS - 1):
        field = sweep2d(field)
    residual = forcing - operate2d(field, screen, scale, nz)
    correction = vcycle2d(restrict2d(residual, ny, nz), level_index + 1, screens, shapes)
    field = field + prolong2d(correction, ny, nz)
    for _ in range(SWEEPS):
        field = sweep2d(field)
    return field


def coarse_solve(f, rho2, ny, nz):
    rho3 = restrict2d(rho2, ny, nz)
    screens = [None, None, screen_weight * rho2, screen_weight * rho3]
    shapes = [None, None, (ny, nz), (ny // 2, nz // 2)]
    return vcycle2d(f, 2, screens, shapes)


def splat(packed):
    tiles, _, slots = packed.shape
    centers = jnp.arange(BRICK, dtype=jnp.float32) + 0.5
    wx, wy, wz = [
        jnp.maximum(0.0, 1.0 - jnp.abs(packed[:, row, None, :] - centers[None, :, None]))
        for row in range(3)
    ]
    planar = (wx[:, :, None, :] * wy[:, None, :, :]).reshape(tiles, BRICK * BRICK, slots)
    loaded = (packed[:, 3:7, None, :] * wz[:, None, :, :]).reshape(tiles, 4 * BRICK, slots)
    partials = jnp.einsum("tbs,tas->tba", loaded, planar, precision=lax.Precision.HIGH)
    brick_total = CX // BRICK * (CY // BRICK) * (CZ // BRICK)
    brick_row = packed[:, 7, :brick_total]
    numbers = lax.broadcasted_iota(jnp.float32, (tiles, brick_total), 1)
    onehot = (brick_row == numbers).astype(jnp.float32)
    sums = jnp.einsum("tk,tba->kba", onehot, partials, precision=lax.Precision.HIGH)
    return sums


def gather_all(block, space_count, sub_count):
    channels, nx, ny, nz = block.shape
    devices = space_count * sub_count
    flat = block.reshape(1, channels * nx, ny * nz)
    sent = jnp.broadcast_to(flat, (devices,) + flat.shape[1:])
    every = lax.all_to_all(sent, ("space", "sub"), 0, 0, tiled=True)
    every = every.reshape(space_count, sub_count, channels, nx, ny * nz)
    every = every.transpose(2, 0, 3, 1, 4)
    return every.reshape(channels, space_count * nx, sub_count * ny * nz)


def to_grid(sums):
    shaped = sums.reshape(CX // BRICK, CY // BRICK, CZ // BRICK, 4, BRICK, BRICK, BRICK)
    return shaped.transpose(3, 0, 5, 1, 6, 2, 4).reshape(4, CX, CY, CZ)


def on_device(offsets, normals, density, tile_brick, tile_count):
    space_count = lax.axis_size("space")
    sub_count = lax.axis_size("sub")
    devices = space_count * sub_count
    tiles_each = offsets.shape[4]
    slot_total = offsets.shape[6]

    slot_numbers = lax.broadcasted_iota(jnp.int32, (devices, tiles_each, 1, slot_total), 3)
    live = (slot_numbers < tile_count.reshape(devices, tiles_each, 1, 1)).astype(jnp.float32)
    samples = jnp.concatenate(
        [
            normals.reshape(devices, tiles_each, 3, slot_total),
            density.reshape(devices, tiles_each, 1, slot_total),
        ],
        axis=2,
    ) * live
    brick_row = jnp.broadcast_to(
        tile_brick.reshape(devices, tiles_each, 1, 1).astype(jnp.float32),
        (devices, tiles_each, 1, slot_total),
    )
    packed = jnp.concatenate(
        [offsets.reshape(devices, tiles_each, 3, slot_total), samples, brick_row], axis=2
    )
    received = lax.all_to_all(packed, ("space", "sub"), 0, 0, tiled=True)
    sums = splat(received.reshape(devices * tiles_each, 8, slot_total))
    grid = to_grid(sums)
    density_field = grid[3]

    h0 = HALO0
    g = exchange(grid, h0, 1, 2)
    vx, vy, vz, rho0 = g[0], g[1], g[2], g[3]
    mask0 = inside_mask(CX, CY, CZ, h0)
    hf = h0 - 1
    vzc = jnp.pad(crop(vz, h0, hf), ((0, 0), (0, 0), (1, 1)))
    change = vx[2:, 1:-1] - vx[:-2, 1:-1] + (vy[1:-1, 2:] - vy[1:-1, :-2])
    change = change + (vzc[:, :, 2:] - vzc[:, :, :-2])
    m0 = crop(mask0, h0, hf)
    f0 = -0.5 * change * m0
    screen0 = screen_weight * crop(rho0, h0, hf)
    diag0 = 6.0 + screen0
    u = relax_weight * f0 / diag0 * m0
    u = sweep_ext(u, hf, f0, screen0, diag0, m0, 1.0)
    hu0 = hf - 1
    residual0 = crop(f0, hf, 0) - operate_ext(
        crop(u, hu0, 1), crop(screen0, hf, 0), 1.0
    )

    h1 = HALO1
    f1 = restrict(residual0)
    rho1 = restrict(density_field)
    nx1, ny1, nz1 = f1.shape
    both = exchange(jnp.stack([f1, rho1]), h1, 1, 2)
    f1e, rho1e = both[0], both[1]
    mask1 = inside_mask(nx1, ny1, nz1, h1)
    scale1 = 0.25
    screen1 = screen_weight * rho1e
    diag1 = 6.0 * scale1 + screen1
    u1 = relax_weight * f1e / diag1 * mask1
    u1 = sweep_ext(u1, h1, f1e, screen1, diag1, mask1, scale1)
    hu1 = h1 - 1
    residual1 = crop(f1e, h1, 0) - operate_ext(crop(u1, hu1, 1), crop(screen1, h1, 0), scale1)

    f2 = restrict(residual1)
    nx2, ny2, nz2 = f2.shape

    rho2 = restrict(rho1)
    both2 = gather_all(jnp.stack([f2, rho2]), space_count, sub_count)
    c2g = coarse_solve(both2[0], both2[1], sub_count * ny2, nz2)
    hc2 = (hu1 + 1) // 2
    c2p = jnp.pad(c2g, ((hc2, hc2), (hc2 * nz2, hc2 * nz2)))
    c2 = lax.dynamic_slice(
        c2p,
        (lax.axis_index("space") * nx2, lax.axis_index("sub") * ny2 * nz2),
        (nx2 + 2 * hc2, (ny2 + 2 * hc2) * nz2),
    ).reshape(nx2 + 2 * hc2, ny2 + 2 * hc2, nz2)

    u1 = u1 + crop(prolong(c2), 2 * hc2, hu1)
    hcur = hu1
    while hcur > 1:
        u1 = sweep_ext(
            u1,
            hcur,
            crop(f1e, h1, hcur),
            crop(screen1, h1, hcur),
            crop(diag1, h1, hcur),
            crop(mask1, h1, hcur),
            scale1,
        )
        hcur -= 1
    c1 = u1

    u = u + crop(prolong(c1), 2, hu0)
    hcur = hu0
    for _ in range(SWEEPS):
        u = sweep_ext(
            u,
            hcur,
            crop(f0, hf, hcur),
            crop(screen0, hf, hcur),
            crop(diag0, hf, hcur),
            crop(m0, hf, hcur),
            1.0,
        )
        hcur -= 1
    indicator = crop(u, hcur, 0)
    return (indicator, density_field)


def solution(mesh):
    placed = (
        P("space", "sub", None, None, None, None, None),
        P("space", "sub", None, None, None, None, None),
        P("space", "sub", None, None, None, None),
        P("space", "sub", None, None, None),
        P("space", "sub", None, None, None),
    )
    return jax.shard_map(
        on_device,
        mesh=mesh,
        in_specs=placed,
        out_specs=(P("space", "sub", None), P("space", "sub", None)),
        check_vma=False,
    )
```
